128 devices in a mesh: row: 8 (over y, core), col: 16 (over z, x).
Axes of the slice: x: 4, y: 4, z: 4, core: 2. Of those that a mesh axis runs over, the one named last changes fastest.
Arguments:
- mock_maps: bfloat16 [1024, 163840], P('col', 'row'), may hold values from -6 to 6
- window_blocks: int32 [4], replicated, may hold values from 0 to 127, as said below
- kept_tiles: int32 [128, 4], P(('row', 'col')), may hold values from 0 to 1, as said below
- taper_index: int32 [128, 4], P(('row', 'col')), may hold values from 0 to 3, as said below
- taper_table: float32 [4], replicated, may hold values from 0.25 to 2
Outputs:
- covariance: bfloat16 [163840, 5120], P(('row', 'col'))
The draws below stay inside these ranges and needn't reach their ends.
Inputs may be any that keep to these rules, and one draw needn't show every extreme that they name: `window_blocks`: the entries are distinct feature blocks; the first and the last feature block are always among them. `kept_tiles`: A tile whose row block is its own window column block is always kept. `taper_index`: A tile whose row block is its own window column block takes entry 0.
All inputs are finite; a program needn't handle non-finite values.
Results may differ from the reference program's by a relative error of at most 0.001.
Values may be sent and summed in bfloat16 or wider, within the bound.
No kernel may reach another device: no remote copies, remote signals or barrier semaphores. Data moves between devices by JAX's collectives and lax.ppermute only.
A program may use at most 128 MiB of HBM per device.

```python
import math
import jax
import jax.numpy as jnp
from jax import lax

FB = 1280
WINDOW = 4
NSEP = 4
MOCKS = 1024
NBLK = 128
FEATURES = 163840


def layout_draw(key):
    middle = (jax.random.permutation(jax.random.fold_in(key, 13), NBLK - 2)[:WINDOW - 2] + 1).astype(jnp.int32)
    ends = jnp.array([0, NBLK - 1], dtype=jnp.int32)
    chosen = jnp.concatenate([ends, middle]).astype(jnp.int32)
    order = jax.random.permutation(jax.random.fold_in(key, 14), WINDOW)
    window_ids = chosen[order].astype(jnp.int32)
    separation = jax.random.randint(jax.random.fold_in(key, 12), (NBLK, WINDOW), 0, 2 * NSEP).astype(jnp.int32)
    row_ids = jnp.arange(NBLK, dtype=jnp.int32)[:, None]
    separation = jnp.where(row_ids == window_ids[None, :], 0, separation).astype(jnp.int32)
    return (window_ids, separation)


def draw_window_blocks(key, part):
    return layout_draw(key)[0]


def draw_kept_tiles(key, part):
    return (layout_draw(key)[1] < NSEP).astype(jnp.int32)


def draw_taper_index(key, part):
    return (layout_draw(key)[1] % NSEP).astype(jnp.int32)


def block_levels(stream_key, extent, split, least, high):
    loudness = 1.0
    for position, shards_of in split:
        heights = jax.random.uniform(jax.random.fold_in(jax.random.fold_in(stream_key, 6), position), (shards_of,), jnp.float32, least / len(split), high / len(split))
        loudness = loudness * jnp.repeat(jnp.exp(heights), extent[position] // shards_of).reshape((-1,) + (1,) * (len(extent) - 1 - position))
    return loudness


def scatter_about(own_key, extent, width, most, pieces=(), kind=jnp.bfloat16):
    entries = jax.random.normal(own_key, extent, jnp.float32) * width
    if len(pieces) > 0:
        entries = block_levels(own_key, extent, pieces, -0.22, 0.18) * entries
    return jnp.clip(entries, min=-most, max=most).astype(kind)


def setup_inputs(seed: int = 0) -> dict:
    seeds = jax.random.split(jax.random.key(seed), 6)
    mock_maps = scatter_about(seeds[0], (MOCKS, FEATURES), 1.0, 6.0, ((0, 16), (1, 8)))
    window_blocks = draw_window_blocks(jax.random.fold_in(seeds[5], 71), 0)
    kept_tiles = draw_kept_tiles(jax.random.fold_in(seeds[5], 71), 0)
    taper_index = draw_taper_index(jax.random.fold_in(seeds[5], 71), 0)
    taper_table = jnp.clip(jnp.exp(jax.random.uniform(seeds[4], (NSEP,), jnp.float32, math.log(0.25), math.log(2.0))), 0.25, 2.0)
    return dict(mock_maps=mock_maps, window_blocks=window_blocks, kept_tiles=kept_tiles, taper_index=taper_index, taper_table=taper_table)


def reference(mock_maps, window_blocks, kept_tiles, taper_index, taper_table):
    mock_count = mock_maps.shape[0]
    mean_all = jnp.sum(mock_maps, axis=0, dtype=jnp.float32) / mock_count
    panel_list = []
    panel_means = []
    for slot in range(WINDOW):
        start = (window_blocks[slot] * FB).astype(jnp.int32)
        panel_list.append(lax.dynamic_slice_in_dim(mock_maps, start, FB, 1).astype(jnp.float32))
        panel_means.append(lax.dynamic_slice_in_dim(mean_all, start, FB, 0))
    panels = jnp.concatenate(panel_list, axis=1)
    panel_mean = jnp.concatenate(panel_means, axis=0)

    def one_block(block_id):
        start = (block_id * FB).astype(jnp.int32)
        rows = lax.dynamic_slice_in_dim(mock_maps, start, FB, 1).astype(jnp.float32)
        row_mean = lax.dynamic_slice_in_dim(mean_all, start, FB, 0)
        products = jnp.dot(rows.T, panels, precision=lax.Precision.HIGHEST)
        weights = taper_table[taper_index[block_id]]
        keep = kept_tiles[block_id]
        weight_cols = jnp.repeat(weights, FB)
        keep_cols = jnp.repeat(keep, FB)
        centred = products - mock_count * row_mean[:, None] * panel_mean[None, :]
        tile_value = weight_cols[None, :] * centred / (mock_count - 1)
        tile_value = jnp.where(keep_cols[None, :] > 0, tile_value, jnp.float32(0.0))
        return tile_value.astype(jnp.bfloat16)

    tiles = lax.map(one_block, jnp.arange(NBLK, dtype=jnp.int32))
    return tiles.reshape(NBLK * FB, WINDOW * FB)
```

```python
import jax
import jax.numpy as jnp
from jax import lax
from jax.sharding import PartitionSpec as P

WINDOW = 4


def per_device(mock_maps, window_blocks, kept_tiles, taper_index, taper_table):
    block_width = mock_maps.shape[1] // lax.axis_size("col")
    local_blocks = mock_maps.shape[1] // block_width
    row = lax.axis_index("row")
    chunks = []
    for slot in range(WINDOW):
        local_id = window_blocks[slot] - row * local_blocks
        mine = (local_id >= 0) & (local_id < local_blocks)
        start = jnp.clip(local_id, 0, local_blocks - 1) * block_width
        piece = lax.dynamic_slice_in_dim(mock_maps, start, block_width, 1)
        chunks.append(jnp.where(mine, piece, jnp.zeros_like(piece)))
    local_panels = lax.psum(jnp.concatenate(chunks, axis=1), "row")
    panels = lax.all_gather(local_panels, "col", axis=0, tiled=True)

    own_block = lax.all_to_all(mock_maps, "col", split_axis=1, concat_axis=0, tiled=True)
    mock_count = own_block.shape[0]
    own_mean = jnp.sum(own_block, axis=0, dtype=jnp.float32) / mock_count
    panel_mean = jnp.sum(panels, axis=0, dtype=jnp.float32) / mock_count
    products = lax.dot_general(
        own_block, panels, (((0,), (0,)), ((), ())), preferred_element_type=jnp.float32
    )
    classes = jnp.arange(taper_table.shape[0], dtype=jnp.int32)
    weights = jnp.sum(
        jnp.where(
            classes[None, :] == taper_index[0][:, None], taper_table[None, :], jnp.float32(0.0)
        ),
        axis=1,
    )
    weight_cols = jnp.repeat(weights, block_width)
    keep_cols = jnp.repeat(kept_tiles[0], block_width)
    centred = products - mock_count * own_mean[:, None] * panel_mean[None, :]
    tile_value = weight_cols[None, :] * centred / (mock_count - 1)
    tile_value = jnp.where(keep_cols[None, :] > 0, tile_value, jnp.float32(0.0))
    return tile_value.astype(jnp.bfloat16)


def solution(mesh):
    in_specs = (P("col", "row"), P(), P(("row", "col"), None), P(("row", "col"), None), P())
    out_specs = P(("row", "col"), None)
    return jax.shard_map(
        per_device, mesh=mesh, in_specs=in_specs, out_specs=out_specs, check_vma=False
    )
```

```python
import jax
import jax.numpy as jnp
from jax import lax
from jax.sharding import PartitionSpec as P

WINDOW = 4


def per_device(mock_maps, window_blocks, kept_tiles, taper_index, taper_table):
    block_width = mock_maps.shape[1] // lax.axis_size("col")
    local_blocks = mock_maps.shape[1] // block_width
    row = lax.axis_index("row")
    chunks = []
    for slot in range(WINDOW):
        local_id = window_blocks[slot] - row * local_blocks
        mine = (local_id >= 0) & (local_id < local_blocks)
        start = jnp.clip(local_id, 0, local_blocks - 1) * block_width
        piece = lax.dynamic_slice_in_dim(mock_maps, start, block_width, 1)
        chunks.append(jnp.where(mine, piece, jnp.zeros_like(piece)))
    local_panels = lax.psum_scatter(
        jnp.concatenate(chunks, axis=1), "row", scatter_dimension=0, tiled=True
    )
    panels = lax.all_gather(local_panels, ("col", "row"), axis=0, tiled=True)

    own_block = lax.all_to_all(mock_maps, "col", split_axis=1, concat_axis=0, tiled=True)
    mock_count = own_block.shape[0]
    own_mean = jnp.sum(own_block, axis=0, dtype=jnp.float32) / mock_count
    panel_mean = jnp.sum(panels, axis=0, dtype=jnp.float32) / mock_count
    products = lax.dot_general(
        own_block.T, panels, (((1,), (0,)), ((), ())), preferred_element_type=jnp.float32
    )
    classes = jnp.arange(taper_table.shape[0], dtype=jnp.int32)
    weights = jnp.sum(
        jnp.where(
            classes[None, :] == taper_index[0][:, None], taper_table[None, :], jnp.float32(0.0)
        ),
        axis=1,
    )
    weight_cols = jnp.repeat(weights, block_width)
    keep_cols = jnp.repeat(kept_tiles[0], block_width)
    centred = products - mock_count * own_mean[:, None] * panel_mean[None, :]
    tile_value = weight_cols[None, :] * centred / (mock_count - 1)
    tile_value = jnp.where(keep_cols[None, :] > 0, tile_value, jnp.float32(0.0))
    return tile_value.astype(jnp.bfloat16)


def solution(mesh):
    in_specs = (P("col", "row"), P(), P(("row", "col"), None), P(("row", "col"), None), P())
    out_specs = P(("row", "col"), None)
    return jax.shard_map(
        per_device, mesh=mesh, in_specs=in_specs, out_specs=out_specs, check_vma=False
    )
```

```python
import functools

import jax
import jax.numpy as jnp
from jax import lax
from jax.experimental import pallas as pl
from jax.experimental.pallas import tpu as pltpu
from jax.sharding import PartitionSpec as P

WINDOW = 4
TILE_N = 512


def tile_kernel(mock_count, a_ref, b_ref, rows_ref, w_ref, keep_ref, o_ref):
    b = b_ref[...]
    prod = jnp.dot(a_ref[...], b, preferred_element_type=jnp.float32)
    ones = jnp.ones((8, b.shape[0]), b.dtype)
    col_sum = jnp.dot(ones, b, preferred_element_type=jnp.float32)[0:1, :]
    centred = prod - rows_ref[...] * (col_sum / mock_count)
    val = w_ref[...] * centred / (mock_count - 1)
    o_ref[...] = jnp.where(keep_ref[...] > 0, val, jnp.float32(0.0)).astype(o_ref.dtype)


def covariance_tiles(own_t, panels, row_sums, weight_cols, keep_cols):
    fb, k = own_t.shape
    n = panels.shape[1]
    return pl.pallas_call(
        functools.partial(tile_kernel, k),
        grid=(n // TILE_N,),
        in_specs=[
            pl.BlockSpec((fb, k), lambda j: (0, 0)),
            pl.BlockSpec((k, TILE_N), lambda j: (0, j)),
            pl.BlockSpec((fb, 1), lambda j: (0, 0)),
            pl.BlockSpec((1, TILE_N), lambda j: (0, j)),
            pl.BlockSpec((1, TILE_N), lambda j: (0, j)),
        ],
        out_specs=pl.BlockSpec((fb, TILE_N), lambda j: (0, j)),
        out_shape=jax.ShapeDtypeStruct((fb, n), jnp.bfloat16),
        compiler_params=pltpu.CompilerParams(vmem_limit_bytes=48 * 1024 * 1024),
        cost_estimate=pl.CostEstimate(
            flops=2 * fb * k * n, bytes_accessed=fb * k * 2 + k * n * 2 + fb * n * 2,
            transcendentals=0,
        ),
    )(own_t, panels, row_sums, weight_cols, keep_cols)


def per_device(mock_maps, window_blocks, kept_tiles, taper_index, taper_table):
    block_width = mock_maps.shape[1] // lax.axis_size("col")
    local_blocks = mock_maps.shape[1] // block_width
    row = lax.axis_index("row")
    chunks = []
    for slot in range(WINDOW):
        local_id = window_blocks[slot] - row * local_blocks
        mine = (local_id >= 0) & (local_id < local_blocks)
        start = jnp.clip(local_id, 0, local_blocks - 1) * block_width
        piece = lax.dynamic_slice_in_dim(mock_maps, start, block_width, 1)
        chunks.append(jnp.where(mine, piece, jnp.zeros_like(piece)))
    local_panels = lax.psum_scatter(
        jnp.concatenate(chunks, axis=1), "row", scatter_dimension=0, tiled=True
    )
    panels = lax.all_gather(local_panels, ("col", "row"), axis=0, tiled=True)

    own_block = lax.all_to_all(mock_maps, "col", split_axis=1, concat_axis=0, tiled=True)
    mock_count = own_block.shape[0]
    row_sums = jnp.sum(own_block, axis=0, dtype=jnp.float32)[:, None]
    classes = jnp.arange(taper_table.shape[0], dtype=jnp.int32)
    weights = jnp.sum(
        jnp.where(
            classes[None, :] == taper_index[0][:, None], taper_table[None, :], jnp.float32(0.0)
        ),
        axis=1,
    )
    weight_cols = jnp.repeat(weights, block_width)[None, :]
    keep_cols = jnp.repeat(kept_tiles[0], block_width)[None, :]
    return covariance_tiles(own_block.T, panels, row_sums, weight_cols, keep_cols)


def solution(mesh):
    in_specs = (P("col", "row"), P(), P(("row", "col"), None), P(("row", "col"), None), P())
    out_specs = P(("row", "col"), None)
    return jax.shard_map(
        per_device, mesh=mesh, in_specs=in_specs, out_specs=out_specs, check_vma=False
    )
```

```python
import functools

import jax
import jax.numpy as jnp
from jax import lax
from jax.experimental import pallas as pl
from jax.experimental.pallas import tpu as pltpu
from jax.sharding import Mesh
from jax.sharding import PartitionSpec as P

WINDOW = 4
TILE_N = 512


def tile_kernel(mock_count, off_ref, a_ref, b_ref, rows_ref, w_ref, keep_ref, *rest):
    o_ref = rest[-1]
    b = b_ref[...]
    prod = jnp.dot(a_ref[...], b, preferred_element_type=jnp.float32)
    ones = jnp.ones((8, b.shape[0]), b.dtype)
    col_sum = jnp.dot(ones, b, preferred_element_type=jnp.float32)[0:1, :]
    centred = prod - rows_ref[...] * (col_sum / mock_count)
    val = w_ref[...] * centred / (mock_count - 1)
    o_ref[...] = jnp.where(keep_ref[...] > 0, val, jnp.float32(0.0)).astype(o_ref.dtype)


def half_tiles(offset, own_t, panels_half, row_sums, weight_cols, keep_cols, prev=None):
    fb, k = own_t.shape
    tiles = panels_half.shape[1] // TILE_N
    n = weight_cols.shape[1]
    in_specs = [
        pl.BlockSpec((fb, k), lambda j, off: (0, 0)),
        pl.BlockSpec((k, TILE_N), lambda j, off: (0, j)),
        pl.BlockSpec((fb, 1), lambda j, off: (0, 0)),
        pl.BlockSpec((1, TILE_N), lambda j, off: (0, off[0] * tiles + j)),
        pl.BlockSpec((1, TILE_N), lambda j, off: (0, off[0] * tiles + j)),
    ]
    args = [offset, own_t, panels_half, row_sums, weight_cols, keep_cols]
    aliases = {}
    if prev is not None:
        in_specs.append(pl.BlockSpec(memory_space=pl.ANY))
        args.append(prev)
        aliases = {len(args) - 1: 0}
    grid_spec = pltpu.PrefetchScalarGridSpec(
        num_scalar_prefetch=1,
        grid=(tiles,),
        in_specs=in_specs,
        out_specs=pl.BlockSpec((fb, TILE_N), lambda j, off: (0, off[0] * tiles + j)),
    )
    return pl.pallas_call(
        functools.partial(tile_kernel, k),
        grid_spec=grid_spec,
        out_shape=jax.ShapeDtypeStruct((fb, n), jnp.bfloat16),
        input_output_aliases=aliases,
        compiler_params=pltpu.CompilerParams(vmem_limit_bytes=48 * 1024 * 1024),
        cost_estimate=pl.CostEstimate(
            flops=2 * fb * k * tiles * TILE_N,
            bytes_accessed=fb * k * 2 + k * tiles * TILE_N * 2 + fb * tiles * TILE_N * 2,
            transcendentals=0,
        ),
    )(*args)


def per_device(mock_maps, window_blocks, kept_tiles, taper_index, taper_table):
    block_width = mock_maps.shape[1] // lax.axis_size("col")
    local_blocks = mock_maps.shape[1] // block_width
    ny = lax.axis_size("y")
    ncore = lax.axis_size("core")
    core = lax.axis_index("core")
    row = lax.axis_index("y") * ncore + core
    chunks = []
    for slot in range(WINDOW):
        local_id = window_blocks[slot] - row * local_blocks
        mine = (local_id >= 0) & (local_id < local_blocks)
        start = jnp.clip(local_id, 0, local_blocks - 1) * block_width
        piece = lax.dynamic_slice_in_dim(mock_maps, start, block_width, 1)
        chunks.append(jnp.where(mine, piece, jnp.zeros_like(piece)))
    local = jnp.concatenate(chunks, axis=1)
    m, n = local.shape
    local = local.reshape(ny, m // ny, ncore, n // ncore).transpose(0, 2, 1, 3)
    local = local.reshape(m * ncore, n // ncore)
    part = lax.psum_scatter(local, ("y", "core"), scatter_dimension=0, tiled=True)
    own_half = lax.all_gather(part, ("col", "y"), axis=0, tiled=True)
    other_half = lax.ppermute(own_half, "core", [(0, 1), (1, 0)])

    own_block = lax.all_to_all(mock_maps, "col", split_axis=1, concat_axis=0, tiled=True)
    row_sums = jnp.sum(own_block, axis=0, dtype=jnp.float32)[:, None]
    classes = jnp.arange(taper_table.shape[0], dtype=jnp.int32)
    weights = jnp.sum(
        jnp.where(
            classes[None, :] == taper_index[0][:, None], taper_table[None, :], jnp.float32(0.0)
        ),
        axis=1,
    )
    weight_cols = jnp.repeat(weights, block_width)[None, :]
    keep_cols = jnp.repeat(kept_tiles[0], block_width)[None, :]
    own_t = own_block.T
    first = half_tiles(
        core.astype(jnp.int32).reshape(1), own_t, own_half, row_sums, weight_cols, keep_cols
    )
    return half_tiles(
        (1 - core).astype(jnp.int32).reshape(1),
        own_t, other_half, row_sums, weight_cols, keep_cols, prev=first,
    )


def solution(mesh):
    rows, cols = mesh.devices.shape
    devices = mesh.devices.reshape(rows // 2, 2, cols)
    split_mesh = Mesh(devices, ("y", "core", "col"))
    feature_rows = ("y", "core", "col")
    in_specs = (P("col", ("y", "core")), P(), P(feature_rows, None), P(feature_rows, None), P())
    out_specs = P(feature_rows, None)
    return jax.shard_map(
        per_device, mesh=split_mesh, in_specs=in_specs, out_specs=out_specs, check_vma=False
    )
```

```python
import functools

import jax
import jax.numpy as jnp
from jax import lax
from jax.experimental import pallas as pl
from jax.experimental.pallas import tpu as pltpu
from jax.sharding import Mesh
from jax.sharding import PartitionSpec as P

WINDOW = 4
TILE_N = 512


def tile_kernel(mock_count, off_ref, a_ref, b_ref, rows_ref, w_ref, keep_ref, *rest):
    o_ref = rest[-1]
    b = b_ref[...]
    prod = jnp.dot(a_ref[...], b, preferred_element_type=jnp.float32)
    ones = jnp.ones((8, b.shape[0]), b.dtype)
    col_sum = jnp.dot(ones, b, preferred_element_type=jnp.float32)[0:1, :]
    centred = prod - rows_ref[...] * (col_sum / mock_count)
    val = w_ref[...] * centred / (mock_count - 1)
    o_ref[...] = jnp.where(keep_ref[...] > 0, val, jnp.float32(0.0)).astype(o_ref.dtype)


def half_tiles(offset, own_t, panels_half, row_sums, weight_cols, keep_cols, prev=None):
    fb, k = own_t.shape
    tiles = panels_half.shape[1] // TILE_N
    n = weight_cols.shape[1]
    in_specs = [
        pl.BlockSpec((fb, k), lambda j, off: (0, 0)),
        pl.BlockSpec((k, TILE_N), lambda j, off: (0, j)),
        pl.BlockSpec((fb, 1), lambda j, off: (0, 0)),
        pl.BlockSpec((1, TILE_N), lambda j, off: (0, off[0] * tiles + j)),
        pl.BlockSpec((1, TILE_N), lambda j, off: (0, off[0] * tiles + j)),
    ]
    args = [offset, own_t, panels_half, row_sums, weight_cols, keep_cols]
    aliases = {}
    if prev is not None:
        in_specs.append(pl.BlockSpec(memory_space=pl.ANY))
        args.append(prev)
        aliases = {len(args) - 1: 0}
    grid_spec = pltpu.PrefetchScalarGridSpec(
        num_scalar_prefetch=1,
        grid=(tiles,),
        in_specs=in_specs,
        out_specs=pl.BlockSpec((fb, TILE_N), lambda j, off: (0, off[0] * tiles + j)),
    )
    return pl.pallas_call(
        functools.partial(tile_kernel, k),
        grid_spec=grid_spec,
        out_shape=jax.ShapeDtypeStruct((fb, n), jnp.bfloat16),
        input_output_aliases=aliases,
        compiler_params=pltpu.CompilerParams(vmem_limit_bytes=48 * 1024 * 1024),
        cost_estimate=pl.CostEstimate(
            flops=2 * fb * k * tiles * TILE_N,
            bytes_accessed=fb * k * 2 + k * tiles * TILE_N * 2 + fb * tiles * TILE_N * 2,
            transcendentals=0,
        ),
    )(*args)


def device_body(mock_maps, window_blocks, kept_tiles, taper_index, taper_table):
    block_width = mock_maps.shape[1] // lax.axis_size("col")
    local_blocks = mock_maps.shape[1] // block_width
    ny = lax.axis_size("y")
    ncore = lax.axis_size("core")
    core = lax.axis_index("core")
    row = lax.axis_index("y") * ncore + core
    chunks = []
    for slot in range(WINDOW):
        local_id = window_blocks[slot] - row * local_blocks
        mine = (local_id >= 0) & (local_id < local_blocks)
        start = jnp.clip(local_id, 0, local_blocks - 1) * block_width
        piece = lax.dynamic_slice_in_dim(mock_maps, start, block_width, 1)
        chunks.append(jnp.where(mine, piece, jnp.zeros_like(piece)))
    local = jnp.concatenate(chunks, axis=1)
    m, n = local.shape
    local = local.reshape(ny, m // ny, ncore, n // ncore).transpose(0, 2, 1, 3)
    local = local.reshape(m * ncore, n // ncore)
    sent = lax.all_to_all(local, ("y", "core"), split_axis=0, concat_axis=0, tiled=True)
    part = jnp.sum(sent.reshape(ny * ncore, m // ny, n // ncore), axis=0, dtype=sent.dtype)
    own_half = lax.all_gather(part, ("col", "y"), axis=0, tiled=True)
    other_half = lax.ppermute(own_half, "core", [(0, 1), (1, 0)])

    own_block = lax.all_to_all(mock_maps, "col", split_axis=1, concat_axis=0, tiled=True)
    row_sums = jnp.sum(own_block, axis=0, dtype=jnp.float32)[:, None]
    classes = jnp.arange(taper_table.shape[0], dtype=jnp.int32)
    weights = jnp.sum(
        jnp.where(
            classes[None, :] == taper_index[0][:, None], taper_table[None, :], jnp.float32(0.0)
        ),
        axis=1,
    )
    weight_cols = jnp.repeat(weights, block_width)[None, :]
    keep_cols = jnp.repeat(kept_tiles[0], block_width)[None, :]
    own_t = own_block.T
    first = half_tiles(
        core.astype(jnp.int32).reshape(1), own_t, own_half, row_sums, weight_cols, keep_cols
    )
    return half_tiles(
        (1 - core).astype(jnp.int32).reshape(1),
        own_t, other_half, row_sums, weight_cols, keep_cols, prev=first,
    )


def solution(mesh):
    rows, cols = mesh.devices.shape
    devices = mesh.devices.reshape(rows // 2, 2, cols)
    split_mesh = Mesh(devices, ("y", "core", "col"))
    feature_rows = ("y", "core", "col")
    in_specs = (P("col", ("y", "core")), P(), P(feature_rows, None), P(feature_rows, None), P())
    out_specs = P(feature_rows, None)
    return jax.shard_map(
        device_body, mesh=split_mesh, in_specs=in_specs, out_specs=out_specs, check_vma=False
    )
```

```python
import functools

import jax
import jax.numpy as jnp
from jax import lax
from jax.experimental import pallas as pl
from jax.experimental.pallas import tpu as pltpu
from jax.sharding import Mesh
from jax.sharding import PartitionSpec as P

WINDOW = 4
TILE_N = 640


def tile_kernel(mock_count, off_ref, a_ref, b_ref, rows_ref, w_ref, keep_ref, *rest):
    o_ref = rest[-1]
    b = b_ref[...]
    prod = jnp.dot(a_ref[...], b, preferred_element_type=jnp.float32)
    ones = jnp.ones((8, b.shape[0]), b.dtype)
    col_sum = jnp.dot(ones, b, preferred_element_type=jnp.float32)[0:1, :]
    centred = prod - rows_ref[...] * (col_sum / mock_count)
    val = centred * w_ref[...]
    o_ref[...] = jnp.where(keep_ref[...] > 0, val, jnp.float32(0.0)).astype(o_ref.dtype)


def half_tiles(offset, own_t, panels_half, row_sums, weight_cols, keep_cols, prev=None):
    fb, k = own_t.shape
    tiles = panels_half.shape[1] // TILE_N
    n = weight_cols.shape[1]
    in_specs = [
        pl.BlockSpec((fb, k), lambda j, off: (0, 0)),
        pl.BlockSpec((k, TILE_N), lambda j, off: (0, j)),
        pl.BlockSpec((fb, 1), lambda j, off: (0, 0)),
        pl.BlockSpec((1, TILE_N), lambda j, off: (0, off[0] + j)),
        pl.BlockSpec((1, TILE_N), lambda j, off: (0, off[0] + j)),
    ]
    args = [offset, own_t, panels_half, row_sums, weight_cols, keep_cols]
    aliases = {}
    if prev is not None:
        in_specs.append(pl.BlockSpec(memory_space=pl.ANY))
        args.append(prev)
        aliases = {len(args) - 1: 0}
    grid_spec = pltpu.PrefetchScalarGridSpec(
        num_scalar_prefetch=1,
        grid=(tiles,),
        in_specs=in_specs,
        out_specs=pl.BlockSpec((fb, TILE_N), lambda j, off: (0, off[0] + j)),
    )
    return pl.pallas_call(
        functools.partial(tile_kernel, k),
        grid_spec=grid_spec,
        out_shape=jax.ShapeDtypeStruct((fb, n), jnp.bfloat16),
        input_output_aliases=aliases,
        compiler_params=pltpu.CompilerParams(vmem_limit_bytes=48 * 1024 * 1024),
        cost_estimate=pl.CostEstimate(
            flops=2 * fb * k * tiles * TILE_N,
            bytes_accessed=fb * k * 2 + k * tiles * TILE_N * 2 + fb * tiles * TILE_N * 2,
            transcendentals=0,
        ),
    )(*args)


def device_body(mock_maps, window_blocks, kept_tiles, taper_index, taper_table):
    block_width = mock_maps.shape[1] // lax.axis_size("col")
    local_blocks = mock_maps.shape[1] // block_width
    ny = lax.axis_size("y")
    ncore = lax.axis_size("core")
    core = lax.axis_index("core")
    row = lax.axis_index("y") * ncore + core
    chunks = []
    for slot in range(WINDOW):
        local_id = window_blocks[slot] - row * local_blocks
        mine = (local_id >= 0) & (local_id < local_blocks)
        start = jnp.clip(local_id, 0, local_blocks - 1) * block_width
        piece = lax.dynamic_slice_in_dim(mock_maps, start, block_width, 1)
        chunks.append(jnp.where(mine, piece, jnp.zeros_like(piece)))
    local = jnp.concatenate(chunks, axis=1)
    m, n = local.shape
    local = local.reshape(ny, m // ny, ncore, n // ncore).transpose(0, 2, 1, 3)
    local = local.reshape(m * ncore, n // ncore)
    sent = lax.all_to_all(local, ("y", "core"), split_axis=0, concat_axis=0, tiled=True)
    part = jnp.sum(sent.reshape(ny * ncore, m // ny, n // ncore), axis=0, dtype=sent.dtype)
    quarter = part.shape[1] // 2
    own_a = lax.all_gather(part[:, :quarter], ("col", "y"), axis=0, tiled=True)
    own_b = lax.all_gather(part[:, quarter:], ("col", "y"), axis=0, tiled=True)
    other_a = lax.ppermute(own_a, "core", [(0, 1), (1, 0)])
    other_b = lax.ppermute(own_b, "core", [(0, 1), (1, 0)])

    own_block = lax.all_to_all(mock_maps, "col", split_axis=1, concat_axis=0, tiled=True)
    row_sums = jnp.sum(own_block, axis=0, dtype=jnp.float32)[:, None]
    classes = jnp.arange(taper_table.shape[0], dtype=jnp.int32)
    weights = jnp.sum(
        jnp.where(
            classes[None, :] == taper_index[0][:, None], taper_table[None, :], jnp.float32(0.0)
        ),
        axis=1,
    )
    mock_count = own_block.shape[0]
    weight_cols = jnp.repeat(weights / (mock_count - 1), block_width)[None, :]
    keep_cols = jnp.repeat(kept_tiles[0], block_width)[None, :]
    own_t = own_block.T
    step = own_a.shape[1] // TILE_N
    mine = core.astype(jnp.int32) * 2 * step
    theirs = (1 - core).astype(jnp.int32) * 2 * step
    out = half_tiles(mine.reshape(1), own_t, own_a, row_sums, weight_cols, keep_cols)
    out = half_tiles(
        (mine + step).reshape(1), own_t, own_b, row_sums, weight_cols, keep_cols, prev=out
    )
    out = half_tiles(theirs.reshape(1), own_t, other_a, row_sums, weight_cols, keep_cols, prev=out)
    return half_tiles(
        (theirs + step).reshape(1), own_t, other_b, row_sums, weight_cols, keep_cols, prev=out
    )


def solution(mesh):
    rows, cols = mesh.devices.shape
    devices = mesh.devices.reshape(rows // 2, 2, cols)
    split_mesh = Mesh(devices, ("y", "core", "col"))
    feature_rows = ("y", "core", "col")
    in_specs = (P("col", ("y", "core")), P(), P(feature_rows, None), P(feature_rows, None), P())
    out_specs = P(feature_rows, None)
    return jax.shard_map(
        device_body, mesh=split_mesh, in_specs=in_specs, out_specs=out_specs, check_vma=False
    )
```

```python
import functools

import jax
import jax.numpy as jnp
from jax import lax
from jax.experimental import pallas as pl
from jax.experimental.pallas import tpu as pltpu
from jax.sharding import Mesh
from jax.sharding import PartitionSpec as P

WINDOW = 4
TILE_N = 512


def tile_kernel(mock_count, off_ref, a_ref, b_ref, rows_ref, w_ref, keep_ref, *rest):
    o_ref = rest[-1]
    b = b_ref[...]
    prod = jnp.dot(a_ref[...], b, preferred_element_type=jnp.float32)
    ones = jnp.ones((8, b.shape[0]), b.dtype)
    col_sum = jnp.dot(ones, b, preferred_element_type=jnp.float32)[0:1, :]
    centred = prod - rows_ref[...] * (col_sum / mock_count)
    val = centred * w_ref[...]
    o_ref[...] = jnp.where(keep_ref[...] > 0, val, jnp.float32(0.0)).astype(o_ref.dtype)


def half_tiles(offset, own_t, panels_half, row_sums, weight_cols, keep_cols, prev=None):
    fb, k = own_t.shape
    tiles = panels_half.shape[1] // TILE_N
    n = weight_cols.shape[1]
    in_specs = [
        pl.BlockSpec((fb, k), lambda j, off: (0, 0)),
        pl.BlockSpec((k, TILE_N), lambda j, off: (0, j)),
        pl.BlockSpec((fb, 1), lambda j, off: (0, 0)),
        pl.BlockSpec((1, TILE_N), lambda j, off: (0, off[0] * tiles + j)),
        pl.BlockSpec((1, TILE_N), lambda j, off: (0, off[0] * tiles + j)),
    ]
    args = [offset, own_t, panels_half, row_sums, weight_cols, keep_cols]
    aliases = {}
    if prev is not None:
        in_specs.append(pl.BlockSpec(memory_space=pl.ANY))
        args.append(prev)
        aliases = {len(args) - 1: 0}
    grid_spec = pltpu.PrefetchScalarGridSpec(
        num_scalar_prefetch=1,
        grid=(tiles,),
        in_specs=in_specs,
        out_specs=pl.BlockSpec((fb, TILE_N), lambda j, off: (0, off[0] * tiles + j)),
    )
    return pl.pallas_call(
        functools.partial(tile_kernel, k),
        grid_spec=grid_spec,
        out_shape=jax.ShapeDtypeStruct((fb, n), jnp.bfloat16),
        input_output_aliases=aliases,
        compiler_params=pltpu.CompilerParams(vmem_limit_bytes=48 * 1024 * 1024),
        cost_estimate=pl.CostEstimate(
            flops=2 * fb * k * tiles * TILE_N,
            bytes_accessed=fb * k * 2 + k * tiles * TILE_N * 2 + fb * tiles * TILE_N * 2,
            transcendentals=0,
        ),
    )(*args)


def device_body(mock_maps, window_blocks, kept_tiles, taper_index, taper_table):
    block_width = mock_maps.shape[1] // lax.axis_size("col")
    local_blocks = mock_maps.shape[1] // block_width
    ny = lax.axis_size("y")
    ncore = lax.axis_size("core")
    core = lax.axis_index("core")
    row = lax.axis_index("y") * ncore + core
    chunks = []
    for slot in range(WINDOW):
        local_id = window_blocks[slot] - row * local_blocks
        mine = (local_id >= 0) & (local_id < local_blocks)
        start = jnp.clip(local_id, 0, local_blocks - 1) * block_width
        piece = lax.dynamic_slice_in_dim(mock_maps, start, block_width, 1)
        chunks.append(jnp.where(mine, piece, jnp.zeros_like(piece)))
    local = jnp.concatenate(chunks, axis=1)
    m, n = local.shape
    local = local.reshape(ny, m // ny, ncore, n // ncore).transpose(0, 2, 1, 3)
    local = local.reshape(m * ncore, n // ncore)
    sent = lax.all_to_all(local, ("y", "core"), split_axis=0, concat_axis=0, tiled=True)
    part = jnp.sum(sent.reshape(ny * ncore, m // ny, n // ncore), axis=0, dtype=sent.dtype)
    part = lax.all_gather(part, "y", axis=0, tiled=True)
    own_half = lax.all_gather(part, "col", axis=0, tiled=True)
    other_half = lax.ppermute(own_half, "core", [(0, 1), (1, 0)])

    own_block = lax.all_to_all(mock_maps, "col", split_axis=1, concat_axis=0, tiled=True)
    row_sums = jnp.sum(own_block, axis=0, dtype=jnp.float32)[:, None]
    classes = jnp.arange(taper_table.shape[0], dtype=jnp.int32)
    weights = jnp.sum(
        jnp.where(
            classes[None, :] == taper_index[0][:, None], taper_table[None, :], jnp.float32(0.0)
        ),
        axis=1,
    )
    mock_count = own_block.shape[0]
    weight_cols = jnp.repeat(weights / (mock_count - 1), block_width)[None, :]
    keep_cols = jnp.repeat(kept_tiles[0], block_width)[None, :]
    own_t = own_block.T
    first = half_tiles(
        core.astype(jnp.int32).reshape(1), own_t, own_half, row_sums, weight_cols, keep_cols
    )
    return half_tiles(
        (1 - core).astype(jnp.int32).reshape(1),
        own_t, other_half, row_sums, weight_cols, keep_cols, prev=first,
    )


def solution(mesh):
    rows, cols = mesh.devices.shape
    devices = mesh.devices.reshape(rows // 2, 2, cols)
    split_mesh = Mesh(devices, ("y", "core", "col"))
    feature_rows = ("y", "core", "col")
    in_specs = (P("col", ("y", "core")), P(), P(feature_rows, None), P(feature_rows, None), P())
    out_specs = P(feature_rows, None)
    return jax.shard_map(
        device_body, mesh=split_mesh, in_specs=in_specs, out_specs=out_specs, check_vma=False
    )
```

```python
import functools

import jax
import jax.numpy as jnp
from jax import lax
from jax.experimental import pallas as pl
from jax.experimental.pallas import tpu as pltpu
from jax.sharding import Mesh
from jax.sharding import PartitionSpec as P

WINDOW = 4
TILE_N = 1280


def tile_kernel(mock_count, off_ref, a_ref, b_ref, rows_ref, w_ref, keep_ref, *rest):
    o_ref = rest[-1]
    b = b_ref[...]
    prod = jnp.dot(a_ref[...], b, preferred_element_type=jnp.float32)
    ones = jnp.ones((8, b.shape[0]), b.dtype)
    col_sum = jnp.dot(ones, b, preferred_element_type=jnp.float32)[0:1, :]
    centred = prod - rows_ref[...] * (col_sum / mock_count)
    val = centred * w_ref[...]
    o_ref[...] = jnp.where(keep_ref[...] > 0, val, jnp.float32(0.0)).astype(o_ref.dtype)


def half_tiles(offset, own_t, panels_half, row_sums, weight_cols, keep_cols, prev=None):
    fb, k = own_t.shape
    tiles = panels_half.shape[1] // TILE_N
    n = weight_cols.shape[1]
    in_specs = [
        pl.BlockSpec((fb, k), lambda j, off: (0, 0)),
        pl.BlockSpec((k, TILE_N), lambda j, off: (0, j)),
        pl.BlockSpec((fb, 1), lambda j, off: (0, 0)),
        pl.BlockSpec((1, TILE_N), lambda j, off: (0, off[0] * tiles + j)),
        pl.BlockSpec((1, TILE_N), lambda j, off: (0, off[0] * tiles + j)),
    ]
    args = [offset, own_t, panels_half, row_sums, weight_cols, keep_cols]
    aliases = {}
    if prev is not None:
        in_specs.append(pl.BlockSpec(memory_space=pl.ANY))
        args.append(prev)
        aliases = {len(args) - 1: 0}
    grid_spec = pltpu.PrefetchScalarGridSpec(
        num_scalar_prefetch=1,
        grid=(tiles,),
        in_specs=in_specs,
        out_specs=pl.BlockSpec((fb, TILE_N), lambda j, off: (0, off[0] * tiles + j)),
    )
    return pl.pallas_call(
        functools.partial(tile_kernel, k),
        grid_spec=grid_spec,
        out_shape=jax.ShapeDtypeStruct((fb, n), jnp.bfloat16),
        input_output_aliases=aliases,
        compiler_params=pltpu.CompilerParams(vmem_limit_bytes=48 * 1024 * 1024),
        cost_estimate=pl.CostEstimate(
            flops=2 * fb * k * tiles * TILE_N,
            bytes_accessed=fb * k * 2 + k * tiles * TILE_N * 2 + fb * tiles * TILE_N * 2,
            transcendentals=0,
        ),
    )(*args)


def device_body(mock_maps, window_blocks, kept_tiles, taper_index, taper_table):
    block_width = mock_maps.shape[1] // lax.axis_size("col")
    local_blocks = mock_maps.shape[1] // block_width
    ny = lax.axis_size("y")
    ncore = lax.axis_size("core")
    core = lax.axis_index("core")
    row = lax.axis_index("y") * ncore + core
    chunks = []
    for slot in range(WINDOW):
        local_id = window_blocks[slot] - row * local_blocks
        mine = (local_id >= 0) & (local_id < local_blocks)
        start = jnp.clip(local_id, 0, local_blocks - 1) * block_width
        piece = lax.dynamic_slice_in_dim(mock_maps, start, block_width, 1)
        chunks.append(jnp.where(mine, piece, jnp.zeros_like(piece)))
    local = jnp.concatenate(chunks, axis=1)
    m, n = local.shape
    local = local.reshape(ny, m // ny, ncore, n // ncore).transpose(0, 2, 1, 3)
    local = local.reshape(m * ncore, n // ncore)
    sent = lax.all_to_all(local, ("y", "core"), split_axis=0, concat_axis=0, tiled=True)
    part = jnp.sum(sent.reshape(ny * ncore, m // ny, n // ncore), axis=0, dtype=sent.dtype)
    own_half = lax.all_gather(part, ("col", "y"), axis=0, tiled=True)
    other_half = lax.ppermute(own_half, "core", [(0, 1), (1, 0)])

    own_block = lax.all_to_all(mock_maps, "col", split_axis=1, concat_axis=0, tiled=True)
    row_sums = jnp.sum(own_block, axis=0, dtype=jnp.float32)[:, None]
    classes = jnp.arange(taper_table.shape[0], dtype=jnp.int32)
    weights = jnp.sum(
        jnp.where(
            classes[None, :] == taper_index[0][:, None], taper_table[None, :], jnp.float32(0.0)
        ),
        axis=1,
    )
    mock_count = own_block.shape[0]
    weight_cols = jnp.repeat(weights / (mock_count - 1), block_width)[None, :]
    keep_cols = jnp.repeat(kept_tiles[0], block_width)[None, :]
    own_t = own_block.T
    first = half_tiles(
        core.astype(jnp.int32).reshape(1), own_t, own_half, row_sums, weight_cols, keep_cols
    )
    return half_tiles(
        (1 - core).astype(jnp.int32).reshape(1),
        own_t, other_half, row_sums, weight_cols, keep_cols, prev=first,
    )


def solution(mesh):
    rows, cols = mesh.devices.shape
    devices = mesh.devices.reshape(rows // 2, 2, cols)
    split_mesh = Mesh(devices, ("y", "core", "col"))
    feature_rows = ("y", "core", "col")
    in_specs = (P("col", ("y", "core")), P(), P(feature_rows, None), P(feature_rows, None), P())
    out_specs = P(feature_rows, None)
    return jax.shard_map(
        device_body, mesh=split_mesh, in_specs=in_specs, out_specs=out_specs, check_vma=False
    )
```

```python
import functools

import jax
import jax.numpy as jnp
from jax import lax
from jax.experimental import pallas as pl
from jax.experimental.pallas import tpu as pltpu
from jax.sharding import Mesh
from jax.sharding import PartitionSpec as P

WINDOW = 4
TILE_N = 1280


def tile_kernel(mock_count, off_ref, a_ref, b_ref, rows_ref, w_ref, keep_ref, *rest):
    o_ref = rest[-1]
    b = b_ref[...]
    prod = jnp.dot(a_ref[...], b, preferred_element_type=jnp.float32)
    ones = jnp.ones((8, b.shape[0]), b.dtype)
    col_sum = jnp.dot(ones, b, preferred_element_type=jnp.float32)[0:1, :]
    centred = prod - rows_ref[...] * (col_sum / mock_count)
    val = centred * w_ref[...]
    o_ref[...] = jnp.where(keep_ref[...] > 0, val, jnp.float32(0.0)).astype(o_ref.dtype)


def half_tiles(offset, own_t, panels_half, row_sums, weight_cols, keep_cols, prev=None):
    fb, k = own_t.shape
    tiles = panels_half.shape[1] // TILE_N
    n = weight_cols.shape[1]
    in_specs = [
        pl.BlockSpec((fb, k), lambda j, off: (0, 0)),
        pl.BlockSpec((k, TILE_N), lambda j, off: (0, j)),
        pl.BlockSpec((fb, 1), lambda j, off: (0, 0)),
        pl.BlockSpec((1, TILE_N), lambda j, off: (0, off[0] * tiles + j)),
        pl.BlockSpec((1, TILE_N), lambda j, off: (0, off[0] * tiles + j)),
    ]
    args = [offset, own_t, panels_half, row_sums, weight_cols, keep_cols]
    aliases = {}
    if prev is not None:
        in_specs.append(pl.BlockSpec(memory_space=pl.ANY))
        args.append(prev)
        aliases = {len(args) - 1: 0}
    grid_spec = pltpu.PrefetchScalarGridSpec(
        num_scalar_prefetch=1,
        grid=(tiles,),
        in_specs=in_specs,
        out_specs=pl.BlockSpec((fb, TILE_N), lambda j, off: (0, off[0] * tiles + j)),
    )
    return pl.pallas_call(
        functools.partial(tile_kernel, k),
        grid_spec=grid_spec,
        out_shape=jax.ShapeDtypeStruct((fb, n), jnp.bfloat16),
        input_output_aliases=aliases,
        compiler_params=pltpu.CompilerParams(vmem_limit_bytes=48 * 1024 * 1024),
        cost_estimate=pl.CostEstimate(
            flops=2 * fb * k * tiles * TILE_N,
            bytes_accessed=fb * k * 2 + k * tiles * TILE_N * 2 + fb * tiles * TILE_N * 2,
            transcendentals=0,
        ),
    )(*args)


def device_body(mock_maps, window_blocks, kept_tiles, taper_index, taper_table):
    block_width = mock_maps.shape[1] // lax.axis_size("col")
    local_blocks = mock_maps.shape[1] // block_width
    ny = lax.axis_size("y")
    ncore = lax.axis_size("core")
    core = lax.axis_index("core")
    row = lax.axis_index("y") * ncore + core
    chunks = []
    for slot in range(WINDOW):
        local_id = window_blocks[slot] - row * local_blocks
        mine = (local_id >= 0) & (local_id < local_blocks)
        start = jnp.clip(local_id, 0, local_blocks - 1) * block_width
        piece = lax.dynamic_slice_in_dim(mock_maps, start, block_width, 1)
        chunks.append(jnp.where(mine, piece, jnp.zeros_like(piece)))
    local = jnp.concatenate(chunks, axis=1)
    m, n = local.shape
    local = local.reshape(ny, m // ny, ncore, n // ncore).transpose(0, 2, 1, 3)
    local = local.reshape(m * ncore, n // ncore)
    sent = lax.all_to_all(local, ("y", "core"), split_axis=0, concat_axis=0, tiled=True)
    part = jnp.sum(sent.reshape(ny * ncore, m // ny, n // ncore), axis=0, dtype=sent.dtype)
    own_half = lax.all_gather(part, ("y", "col"), axis=0, tiled=True)
    other_half = lax.ppermute(own_half, "core", [(0, 1), (1, 0)])

    own_block = lax.all_to_all(mock_maps, "col", split_axis=1, concat_axis=0, tiled=True)
    row_sums = jnp.sum(own_block, axis=0, dtype=jnp.float32)[:, None]
    classes = jnp.arange(taper_table.shape[0], dtype=jnp.int32)
    weights = jnp.sum(
        jnp.where(
            classes[None, :] == taper_index[0][:, None], taper_table[None, :], jnp.float32(0.0)
        ),
        axis=1,
    )
    mock_count = own_block.shape[0]
    weight_cols = jnp.repeat(weights / (mock_count - 1), block_width)[None, :]
    keep_cols = jnp.repeat(kept_tiles[0], block_width)[None, :]
    ncol = lax.axis_size("col")
    fb = own_block.shape[1]
    own_t = own_block.reshape(ncol, ny, mock_count // (ncol * ny), fb)
    own_t = own_t.transpose(3, 1, 0, 2).reshape(fb, mock_count)
    first = half_tiles(
        core.astype(jnp.int32).reshape(1), own_t, own_half, row_sums, weight_cols, keep_cols
    )
    return half_tiles(
        (1 - core).astype(jnp.int32).reshape(1),
        own_t, other_half, row_sums, weight_cols, keep_cols, prev=first,
    )


def solution(mesh):
    rows, cols = mesh.devices.shape
    devices = mesh.devices.reshape(rows // 2, 2, cols)
    split_mesh = Mesh(devices, ("y", "core", "col"))
    feature_rows = ("y", "core", "col")
    in_specs = (P("col", ("y", "core")), P(), P(feature_rows, None), P(feature_rows, None), P())
    out_specs = P(feature_rows, None)
    return jax.shard_map(
        device_body, mesh=split_mesh, in_specs=in_specs, out_specs=out_specs, check_vma=False
    )
```

```python
import functools

import jax
import jax.numpy as jnp
from jax import lax
from jax.experimental import pallas as pl
from jax.experimental.pallas import tpu as pltpu
from jax.sharding import Mesh
from jax.sharding import PartitionSpec as P

WINDOW = 4
TILE_N = 1280


def tile_kernel(mock_count, off_ref, a_ref, b_ref, rows_ref, w_ref, keep_ref, *rest):
    o_ref = rest[-1]
    b = b_ref[...]
    prod = jnp.dot(a_ref[...], b, preferred_element_type=jnp.float32)
    ones = jnp.ones((8, b.shape[0]), b.dtype)
    col_sum = jnp.dot(ones, b, preferred_element_type=jnp.float32)[0:1, :]
    centred = prod - rows_ref[...] * (col_sum / mock_count)
    val = centred * w_ref[...]
    o_ref[...] = jnp.where(keep_ref[...] > 0, val, jnp.float32(0.0)).astype(o_ref.dtype)


def half_tiles(offset, own_t, panels_half, row_sums, weight_cols, keep_cols, prev=None):
    fb, k = own_t.shape
    tiles = panels_half.shape[1] // TILE_N
    n = weight_cols.shape[1]
    in_specs = [
        pl.BlockSpec((fb, k), lambda j, off: (0, 0)),
        pl.BlockSpec((k, TILE_N), lambda j, off: (0, j)),
        pl.BlockSpec((fb, 1), lambda j, off: (0, 0)),
        pl.BlockSpec((1, TILE_N), lambda j, off: (0, off[0] * tiles + j)),
        pl.BlockSpec((1, TILE_N), lambda j, off: (0, off[0] * tiles + j)),
    ]
    args = [offset, own_t, panels_half, row_sums, weight_cols, keep_cols]
    aliases = {}
    if prev is not None:
        in_specs.append(pl.BlockSpec(memory_space=pl.ANY))
        args.append(prev)
        aliases = {len(args) - 1: 0}
    grid_spec = pltpu.PrefetchScalarGridSpec(
        num_scalar_prefetch=1,
        grid=(tiles,),
        in_specs=in_specs,
        out_specs=pl.BlockSpec((fb, TILE_N), lambda j, off: (0, off[0] * tiles + j)),
    )
    return pl.pallas_call(
        functools.partial(tile_kernel, k),
        grid_spec=grid_spec,
        out_shape=jax.ShapeDtypeStruct((fb, n), jnp.bfloat16),
        input_output_aliases=aliases,
        compiler_params=pltpu.CompilerParams(vmem_limit_bytes=48 * 1024 * 1024),
        cost_estimate=pl.CostEstimate(
            flops=2 * fb * k * tiles * TILE_N,
            bytes_accessed=fb * k * 2 + k * tiles * TILE_N * 2 + fb * tiles * TILE_N * 2,
            transcendentals=0,
        ),
    )(*args)


def device_body(mock_maps, window_blocks, kept_tiles, taper_index, taper_table):
    block_width = mock_maps.shape[1] // lax.axis_size("col")
    local_blocks = mock_maps.shape[1] // block_width
    ny = lax.axis_size("y")
    ncore = lax.axis_size("core")
    core = lax.axis_index("core")
    row = lax.axis_index("y") * ncore + core
    chunks = []
    for slot in range(WINDOW):
        local_id = window_blocks[slot] - row * local_blocks
        mine = (local_id >= 0) & (local_id < local_blocks)
        start = jnp.clip(local_id, 0, local_blocks - 1) * block_width
        piece = lax.dynamic_slice_in_dim(mock_maps, start, block_width, 1)
        chunks.append(jnp.where(mine, piece, jnp.zeros_like(piece)))
    per_half = WINDOW // ncore
    halves = [
        jnp.concatenate(chunks[hh * per_half:(hh + 1) * per_half], axis=1) for hh in range(ncore)
    ]
    m = mock_maps.shape[0]
    rows_each = m // ny
    local = jnp.stack(
        [halves[hh][yy * rows_each:(yy + 1) * rows_each] for yy in range(ny) for hh in range(ncore)]
    )
    sent = lax.all_to_all(local, ("y", "core"), split_axis=0, concat_axis=0, tiled=True)
    part = jnp.sum(sent, axis=0, dtype=sent.dtype)
    own_half = lax.all_gather(part, ("y", "col"), axis=0, tiled=True)
    other_half = lax.ppermute(own_half, "core", [(0, 1), (1, 0)])

    own_block = lax.all_to_all(mock_maps, "col", split_axis=1, concat_axis=0, tiled=True)
    row_sums = jnp.sum(own_block, axis=0, dtype=jnp.float32)[:, None]
    classes = jnp.arange(taper_table.shape[0], dtype=jnp.int32)
    weights = jnp.sum(
        jnp.where(
            classes[None, :] == taper_index[0][:, None], taper_table[None, :], jnp.float32(0.0)
        ),
        axis=1,
    )
    mock_count = own_block.shape[0]
    weight_cols = jnp.repeat(weights / (mock_count - 1), block_width)[None, :]
    keep_cols = jnp.repeat(kept_tiles[0], block_width)[None, :]
    ncol = lax.axis_size("col")
    fb = own_block.shape[1]
    own_t = own_block.reshape(ncol, ny, mock_count // (ncol * ny), fb)
    own_t = own_t.transpose(3, 1, 0, 2).reshape(fb, mock_count)
    first = half_tiles(
        core.astype(jnp.int32).reshape(1), own_t, own_half, row_sums, weight_cols, keep_cols
    )
    return half_tiles(
        (1 - core).astype(jnp.int32).reshape(1),
        own_t, other_half, row_sums, weight_cols, keep_cols, prev=first,
    )


def solution(mesh):
    rows, cols = mesh.devices.shape
    devices = mesh.devices.reshape(rows // 2, 2, cols)
    split_mesh = Mesh(devices, ("y", "core", "col"))
    feature_rows = ("y", "core", "col")
    in_specs = (P("col", ("y", "core")), P(), P(feature_rows, None), P(feature_rows, None), P())
    out_specs = P(feature_rows, None)
    return jax.shard_map(
        device_body, mesh=split_mesh, in_specs=in_specs, out_specs=out_specs, check_vma=False
    )
```

```python
import functools

import jax
import jax.numpy as jnp
from jax import lax
from jax.experimental import pallas as pl
from jax.experimental.pallas import tpu as pltpu
from jax.sharding import Mesh
from jax.sharding import PartitionSpec as P

WINDOW = 4
TILE_N = 1280


def tile_kernel(mock_count, off_ref, a_ref, b_ref, rows_ref, w_ref, keep_ref, *rest):
    o_ref = rest[-1]
    b = b_ref[...]
    prod = jnp.dot(a_ref[...], b, preferred_element_type=jnp.float32)
    ones = jnp.ones((8, b.shape[0]), b.dtype)
    col_sum = jnp.dot(ones, b, preferred_element_type=jnp.float32)[0:1, :]
    centred = prod - rows_ref[...] * (col_sum / mock_count)
    val = centred * w_ref[...]
    o_ref[...] = jnp.where(keep_ref[...] > 0, val, jnp.float32(0.0)).astype(o_ref.dtype)


def half_tiles(offset, own_t, panels_half, row_sums, weight_cols, keep_cols, prev=None):
    fb, k = own_t.shape
    tiles = panels_half.shape[1] // TILE_N
    n = weight_cols.shape[1]
    in_specs = [
        pl.BlockSpec((fb, k), lambda j, off: (0, 0)),
        pl.BlockSpec((k, TILE_N), lambda j, off: (0, j)),
        pl.BlockSpec((fb, 1), lambda j, off: (0, 0)),
        pl.BlockSpec((1, TILE_N), lambda j, off: (0, off[0] * tiles + j)),
        pl.BlockSpec((1, TILE_N), lambda j, off: (0, off[0] * tiles + j)),
    ]
    args = [offset, own_t, panels_half, row_sums, weight_cols, keep_cols]
    aliases = {}
    if prev is not None:
        in_specs.append(pl.BlockSpec(memory_space=pl.ANY))
        args.append(prev)
        aliases = {len(args) - 1: 0}
    grid_spec = pltpu.PrefetchScalarGridSpec(
        num_scalar_prefetch=1,
        grid=(tiles,),
        in_specs=in_specs,
        out_specs=pl.BlockSpec((fb, TILE_N), lambda j, off: (0, off[0] * tiles + j)),
    )
    return pl.pallas_call(
        functools.partial(tile_kernel, k),
        grid_spec=grid_spec,
        out_shape=jax.ShapeDtypeStruct((fb, n), jnp.bfloat16),
        input_output_aliases=aliases,
        compiler_params=pltpu.CompilerParams(vmem_limit_bytes=48 * 1024 * 1024),
        cost_estimate=pl.CostEstimate(
            flops=2 * fb * k * tiles * TILE_N,
            bytes_accessed=fb * k * 2 + k * tiles * TILE_N * 2 + fb * tiles * TILE_N * 2,
            transcendentals=0,
        ),
    )(*args)


def device_body(mock_maps, window_blocks, kept_tiles, taper_index, taper_table):
    block_width = mock_maps.shape[1] // lax.axis_size("col")
    local_blocks = mock_maps.shape[1] // block_width
    ny = lax.axis_size("y")
    ncore = lax.axis_size("core")
    core = lax.axis_index("core")
    row = lax.axis_index("y") * ncore + core
    blocks3 = mock_maps.reshape(mock_maps.shape[0], local_blocks, block_width)
    local_ids = window_blocks - row * local_blocks
    onehot = jnp.arange(local_blocks, dtype=jnp.int32)[None, :] == local_ids[:, None]
    picked = jnp.sum(
        jnp.where(onehot[None, :, :, None], blocks3[:, None, :, :], jnp.zeros((), blocks3.dtype)),
        axis=2,
        dtype=blocks3.dtype,
    )
    chunks = [picked[:, slot, :] for slot in range(WINDOW)]
    per_half = WINDOW // ncore
    halves = [
        jnp.concatenate(chunks[hh * per_half:(hh + 1) * per_half], axis=1) for hh in range(ncore)
    ]
    m = mock_maps.shape[0]
    rows_each = m // ny
    local = jnp.stack(
        [halves[hh][yy * rows_each:(yy + 1) * rows_each] for yy in range(ny) for hh in range(ncore)]
    )
    sent = lax.all_to_all(local, ("y", "core"), split_axis=0, concat_axis=0, tiled=True)
    part = jnp.sum(sent, axis=0, dtype=sent.dtype)
    own_half = lax.all_gather(part, ("y", "col"), axis=0, tiled=True)
    other_half = lax.ppermute(own_half, "core", [(0, 1), (1, 0)])

    own_block = lax.all_to_all(mock_maps, "col", split_axis=1, concat_axis=0, tiled=True)
    row_sums = jnp.sum(own_block, axis=0, dtype=jnp.float32)[:, None]
    classes = jnp.arange(taper_table.shape[0], dtype=jnp.int32)
    weights = jnp.sum(
        jnp.where(
            classes[None, :] == taper_index[0][:, None], taper_table[None, :], jnp.float32(0.0)
        ),
        axis=1,
    )
    mock_count = own_block.shape[0]
    weight_cols = jnp.repeat(weights / (mock_count - 1), block_width)[None, :]
    keep_cols = jnp.repeat(kept_tiles[0], block_width)[None, :]
    ncol = lax.axis_size("col")
    fb = own_block.shape[1]
    own_t = own_block.reshape(ncol, ny, mock_count // (ncol * ny), fb)
    own_t = own_t.transpose(3, 1, 0, 2).reshape(fb, mock_count)
    first = half_tiles(
        core.astype(jnp.int32).reshape(1), own_t, own_half, row_sums, weight_cols, keep_cols
    )
    return half_tiles(
        (1 - core).astype(jnp.int32).reshape(1),
        own_t, other_half, row_sums, weight_cols, keep_cols, prev=first,
    )


def solution(mesh):
    rows, cols = mesh.devices.shape
    devices = mesh.devices.reshape(rows // 2, 2, cols)
    split_mesh = Mesh(devices, ("y", "core", "col"))
    feature_rows = ("y", "core", "col")
    in_specs = (P("col", ("y", "core")), P(), P(feature_rows, None), P(feature_rows, None), P())
    out_specs = P(feature_rows, None)
    return jax.shard_map(
        device_body, mesh=split_mesh, in_specs=in_specs, out_specs=out_specs, check_vma=False
    )
```

```python
import functools

import jax
import jax.numpy as jnp
from jax import lax
from jax.experimental import pallas as pl
from jax.experimental.pallas import tpu as pltpu
from jax.sharding import Mesh
from jax.sharding import PartitionSpec as P

WINDOW = 4
TILE_N = 2560
ROW_CHUNK = 128


def tile_kernel(mock_count, off_ref, a_ref, b_ref, rows_ref, w_ref, keep_ref, *rest):
    o_ref = rest[-1]
    b = b_ref[...]
    ones = jnp.ones((8, b.shape[0]), b.dtype)
    col_mean = jnp.dot(ones, b, preferred_element_type=jnp.float32)[0:1, :] / mock_count
    scale = w_ref[...]
    keep = keep_ref[...] > 0
    for r in range(0, a_ref.shape[0], ROW_CHUNK):
        rows = pl.ds(r, ROW_CHUNK)
        prod = jnp.dot(a_ref[rows, :], b, preferred_element_type=jnp.float32)
        centred = prod - rows_ref[rows, :] * col_mean
        val = centred * scale
        o_ref[rows, :] = jnp.where(keep, val, jnp.float32(0.0)).astype(o_ref.dtype)


def half_tiles(offset, own_t, panels_half, row_sums, weight_cols, keep_cols, prev=None):
    fb, k = own_t.shape
    tiles = panels_half.shape[1] // TILE_N
    n = weight_cols.shape[1]
    in_specs = [
        pl.BlockSpec((fb, k), lambda j, off: (0, 0)),
        pl.BlockSpec((k, TILE_N), lambda j, off: (0, j)),
        pl.BlockSpec((fb, 1), lambda j, off: (0, 0)),
        pl.BlockSpec((1, TILE_N), lambda j, off: (0, off[0] * tiles + j)),
        pl.BlockSpec((1, TILE_N), lambda j, off: (0, off[0] * tiles + j)),
    ]
    args = [offset, own_t, panels_half, row_sums, weight_cols, keep_cols]
    aliases = {}
    if prev is not None:
        in_specs.append(pl.BlockSpec(memory_space=pl.ANY))
        args.append(prev)
        aliases = {len(args) - 1: 0}
    grid_spec = pltpu.PrefetchScalarGridSpec(
        num_scalar_prefetch=1,
        grid=(tiles,),
        in_specs=in_specs,
        out_specs=pl.BlockSpec((fb, TILE_N), lambda j, off: (0, off[0] * tiles + j)),
    )
    return pl.pallas_call(
        functools.partial(tile_kernel, k),
        grid_spec=grid_spec,
        out_shape=jax.ShapeDtypeStruct((fb, n), jnp.bfloat16),
        input_output_aliases=aliases,
        compiler_params=pltpu.CompilerParams(vmem_limit_bytes=48 * 1024 * 1024),
        cost_estimate=pl.CostEstimate(
            flops=2 * fb * k * tiles * TILE_N,
            bytes_accessed=fb * k * 2 + k * tiles * TILE_N * 2 + fb * tiles * TILE_N * 2,
            transcendentals=0,
        ),
    )(*args)


def device_body(mock_maps, window_blocks, kept_tiles, taper_index, taper_table):
    block_width = mock_maps.shape[1] // lax.axis_size("col")
    local_blocks = mock_maps.shape[1] // block_width
    ny = lax.axis_size("y")
    ncore = lax.axis_size("core")
    core = lax.axis_index("core")
    row = lax.axis_index("y") * ncore + core
    chunks = []
    for slot in range(WINDOW):
        local_id = window_blocks[slot] - row * local_blocks
        mine = (local_id >= 0) & (local_id < local_blocks)
        start = jnp.clip(local_id, 0, local_blocks - 1) * block_width
        piece = lax.dynamic_slice_in_dim(mock_maps, start, block_width, 1)
        chunks.append(jnp.where(mine, piece, jnp.zeros_like(piece)))
    per_half = WINDOW // ncore
    halves = [
        jnp.concatenate(chunks[hh * per_half:(hh + 1) * per_half], axis=1) for hh in range(ncore)
    ]
    m = mock_maps.shape[0]
    rows_each = m // ny
    local = jnp.stack(
        [halves[hh][yy * rows_each:(yy + 1) * rows_each] for yy in range(ny) for hh in range(ncore)]
    )
    sent = lax.all_to_all(local, ("y", "core"), split_axis=0, concat_axis=0, tiled=True)
    part = jnp.sum(sent, axis=0, dtype=sent.dtype)
    own_half = lax.all_gather(part, ("y", "col"), axis=0, tiled=True)
    other_half = lax.ppermute(own_half, "core", [(0, 1), (1, 0)])

    own_block = lax.all_to_all(mock_maps, "col", split_axis=1, concat_axis=0, tiled=True)
    row_sums = jnp.sum(own_block, axis=0, dtype=jnp.float32)[:, None]
    classes = jnp.arange(taper_table.shape[0], dtype=jnp.int32)
    weights = jnp.sum(
        jnp.where(
            classes[None, :] == taper_index[0][:, None], taper_table[None, :], jnp.float32(0.0)
        ),
        axis=1,
    )
    mock_count = own_block.shape[0]
    weight_cols = jnp.repeat(weights / (mock_count - 1), block_width)[None, :]
    keep_cols = jnp.repeat(kept_tiles[0], block_width)[None, :]
    ncol = lax.axis_size("col")
    fb = own_block.shape[1]
    own_t = own_block.reshape(ncol, ny, mock_count // (ncol * ny), fb)
    own_t = own_t.transpose(3, 1, 0, 2).reshape(fb, mock_count)
    first = half_tiles(
        core.astype(jnp.int32).reshape(1), own_t, own_half, row_sums, weight_cols, keep_cols
    )
    return half_tiles(
        (1 - core).astype(jnp.int32).reshape(1),
        own_t, other_half, row_sums, weight_cols, keep_cols, prev=first,
    )


def solution(mesh):
    rows, cols = mesh.devices.shape
    devices = mesh.devices.reshape(rows // 2, 2, cols)
    split_mesh = Mesh(devices, ("y", "core", "col"))
    feature_rows = ("y", "core", "col")
    in_specs = (P("col", ("y", "core")), P(), P(feature_rows, None), P(feature_rows, None), P())
    out_specs = P(feature_rows, None)
    return jax.shard_map(
        device_body, mesh=split_mesh, in_specs=in_specs, out_specs=out_specs, check_vma=False
    )
```
